128 devices in a mesh: dp: 8 (over x, y_lo), expert: 16 (over z, y_hi, core).
Axes of the slice: x: 4, y: 4 (y_hi: 2, y_lo: 2; y = y_hi * 2 + y_lo), z: 4, core: 2. Of those that a mesh axis runs over, the one named last changes fastest.
Arguments:
- tokens: bfloat16 [16384, 3072], P(('dp', 'expert')), parts along dimension 0, may hold values from -6 to 6
- expert_ids: int32 [16384, 4], P(('dp', 'expert')), parts along dimension 0, may hold values from 0 to 15, as said below
- gate_weights: float32 [16384, 4], P(('dp', 'expert')), parts along dimension 0, may hold values from 0.05 to 0.5
- slot_rows: int32 [128, 16, 64], P(('dp', 'expert')), parts along dimension 0, may hold values from 0 to 128, as said below
- w_in: bfloat16 [16, 3072, 2560], P('expert'), may hold values from -0.109375 to 0.109375
- w_out: bfloat16 [16, 1280, 3072], P('expert'), may hold values from -0.15625 to 0.15625
Outputs:
- mixed: bfloat16 [16384, 3072], P(('dp', 'expert')), parts along dimension 0
The draws below stay inside these ranges and needn't reach their ends.
There are 8 independent parts, one for each index of `dp`. The reference program is written for one: setup_inputs(seed, part) draws one part's arguments, and reference() takes and returns one part's arrays. A program takes and returns all parts, laid end to end along the dimension named above; an argument that names none is the same for every part. Nothing has to cross between parts.
Inputs may be any that keep to these rules, and one draw needn't show every extreme that they name: `expert_ids`: each row names 4 different experts. slot_rows[s, e] lists, in increasing order, the rows of shard s whose tokens name expert e, the first 64 of them, then 128 in the remaining slots; in every draw some expert has all 64 slots filled by every shard.
All inputs are finite; a program needn't handle non-finite values.
Results may differ from the reference program's by a relative error of at most 0.0063.
Values may be sent and summed in bfloat16 or wider, within the bound.
No kernel may reach another device: no remote copies, remote signals or barrier semaphores. Data moves between devices by JAX's collectives and lax.ppermute only.
A program may use at most 128 MiB of HBM per device.

```python
import math
import jax
import jax.numpy as jnp
from jax import lax

D = 3072
FF = 1280
TOP = 4
TOK_DEV = 128
SPECIALIST_TOTAL = 16
TOKENS = 2048
CAP = 64


def routing_tables(key):
    first_key, another_prng_seed = jax.random.split(key, 2)
    specialist_order = jax.random.permutation(first_key, SPECIALIST_TOTAL).astype(jnp.int32)
    gating_jitter = jax.random.randint(another_prng_seed, (SPECIALIST_TOTAL, TOK_DEV, SPECIALIST_TOTAL), 0, 65536).astype(jnp.int32)
    logit_increment = specialist_order * 2048 + jnp.where(specialist_order == SPECIALIST_TOTAL - 1, 1048576, 0).astype(jnp.int32)
    gating_logits = (gating_jitter + logit_increment[None, None, :]) * SPECIALIST_TOTAL + jnp.arange(SPECIALIST_TOTAL, dtype=jnp.int32)[None, None, :]
    chosen_scores, chosen_experts = lax.top_k(gating_logits, TOP)
    chosen_experts = chosen_experts.astype(jnp.int32)
    member = jnp.any(chosen_experts[:, :, :, None] == jnp.arange(SPECIALIST_TOTAL, dtype=jnp.int32)[None, None, None, :], axis=2).astype(jnp.int32)
    position = jnp.cumsum(member, axis=1) - member
    keeping = (member == 1) & (position < CAP)
    slot_index = jnp.arange(CAP, dtype=jnp.int32)
    row_index = jnp.arange(TOK_DEV, dtype=jnp.int32)
    hit = keeping[:, :, :, None] & (position[:, :, :, None] == slot_index[None, None, None, :])
    candidates = jnp.where(hit, row_index[None, :, None, None], TOK_DEV)
    slots = jnp.min(candidates, axis=1).astype(jnp.int32)
    return (chosen_experts.reshape(SPECIALIST_TOTAL * TOK_DEV, TOP), slots)


def draw_expert_ids(key, part):
    chosen_experts, slots = routing_tables(jax.random.fold_in(key, 7))
    return chosen_experts


def draw_slot_rows(key, part):
    chosen_experts, slots = routing_tables(jax.random.fold_in(key, 7))
    return slots


def block_scale(stream_key, extent, pieces, least, top_value):
    gain = 1.0
    for dim, parts in pieces:
        heights = jax.random.uniform(jax.random.fold_in(jax.random.fold_in(stream_key, 6), dim), (parts,), jnp.float32, least / len(pieces), top_value / len(pieces))
        gain = gain * jnp.repeat(jnp.exp(heights), extent[dim] // parts).reshape((-1,) + (1,) * (len(extent) - 1 - dim))
    return gain


def noise(rng, shape, width, most, cuts=(), held_as=jnp.bfloat16):
    level = block_scale(rng, shape, cuts, -0.22, 0.18) if cuts else 1.0
    entries = jax.random.normal(rng, shape, jnp.float32) * width * level
    return jnp.minimum(jnp.maximum(entries, -most), most).astype(held_as)


def setup_inputs(seed: int = 0, part: int = 0) -> dict:
    keys = jax.random.split(jax.random.key(seed), 7)
    part_splits = jax.random.split(jax.random.fold_in(keys[6], part), 7)
    tokens = noise(part_splits[0], (TOKENS, D), 1.0, 6.0, ((0, 16),))
    expert_ids = draw_expert_ids(jax.random.fold_in(jax.random.fold_in(keys[6], part), 71), part)
    gate_weights = jnp.clip(jnp.exp(math.log(0.5) - 2.3025851 * jax.random.uniform(part_splits[2], (TOKENS, TOP), jnp.float32) ** block_scale(part_splits[2], (TOKENS, TOP), ((0, 16),), -0.2, 0.2)), 0.05, 0.5)
    slot_rows = draw_slot_rows(jax.random.fold_in(jax.random.fold_in(keys[6], part), 71), part)
    w_in = noise(keys[4], (SPECIALIST_TOTAL, D, 2 * FF), D ** -0.5, 0.109375, ((0, 16),))
    w_out = noise(keys[5], (SPECIALIST_TOTAL, FF, D), FF ** -0.5, 0.15625, ((0, 16),))
    return {"tokens": tokens, "expert_ids": expert_ids, "gate_weights": gate_weights, "slot_rows": slot_rows, "w_in": w_in, "w_out": w_out}


def reference(tokens, expert_ids, gate_weights, slot_rows, w_in, w_out):
    shards = tokens.reshape(SPECIALIST_TOTAL, TOK_DEV, D)
    occupied = slot_rows < TOK_DEV
    clipped = jnp.minimum(slot_rows, TOK_DEV - 1).astype(jnp.int32)
    ids = expert_ids.reshape(SPECIALIST_TOTAL, TOK_DEV, TOP)
    gates = gate_weights.reshape(SPECIALIST_TOTAL, TOK_DEV, TOP)
    matches = (ids[:, :, :, None] == jnp.arange(SPECIALIST_TOTAL, dtype=jnp.int32)[None, None, None, :]).astype(jnp.float32)
    gate_of = jnp.einsum("stk,stke->set", gates.astype(jnp.float32), matches)
    slot_gate = jnp.where(occupied, jnp.take_along_axis(gate_of, clipped, axis=2), 0.0).astype(jnp.bfloat16)

    def run_expert(expert):
        rows = lax.dynamic_index_in_dim(clipped, expert, axis=1, keepdims=False)
        live = lax.dynamic_index_in_dim(occupied, expert, axis=1, keepdims=False)
        picked_experts = jnp.take_along_axis(shards, rows[:, :, None], axis=1)
        picked_experts = jnp.where(live[:, :, None], picked_experts, jnp.zeros_like(picked_experts)).reshape(SPECIALIST_TOTAL * CAP, D)
        w_first = lax.dynamic_index_in_dim(w_in, expert, axis=0, keepdims=False)
        w_second = lax.dynamic_index_in_dim(w_out, expert, axis=0, keepdims=False)
        projected = jnp.dot(picked_experts, w_first, preferred_element_type=jnp.float32)
        intermediate_activation = (jax.nn.silu(projected[:, :FF]) * projected[:, FF:]).astype(jnp.bfloat16)
        result = jnp.dot(intermediate_activation, w_second, preferred_element_type=jnp.float32).astype(jnp.bfloat16)
        return result.reshape(SPECIALIST_TOTAL, CAP, D)

    expert_out = lax.map(run_expert, jnp.arange(SPECIALIST_TOTAL, dtype=jnp.int32))

    def combine_shard(shard):
        rows = lax.dynamic_index_in_dim(slot_rows, shard, axis=0, keepdims=False).reshape(-1)
        weights = lax.dynamic_index_in_dim(slot_gate, shard, axis=0, keepdims=False).reshape(-1)
        expert_onehot = rows[None, :] == jnp.arange(TOK_DEV, dtype=jnp.int32)[:, None]
        mixing = jnp.where(expert_onehot, weights[None, :], jnp.zeros((), jnp.bfloat16))
        layer_response = lax.dynamic_index_in_dim(expert_out, shard, axis=1, keepdims=False).reshape(SPECIALIST_TOTAL * CAP, D)
        return jnp.dot(mixing, layer_response, preferred_element_type=jnp.float32).astype(jnp.bfloat16)

    mixed = lax.map(combine_shard, jnp.arange(SPECIALIST_TOTAL, dtype=jnp.int32))
    return mixed.reshape(TOKENS, D)
```

```python
import jax
import jax.numpy as jnp
from jax import lax
from jax.sharding import PartitionSpec as P

CHUNKS = 2


def expert_block(rows_in, w_first, w_second):
    features = rows_in.shape[-1]
    hidden_units = w_second.shape[0]
    flat = rows_in.reshape(-1, features)
    projected = jnp.dot(flat, w_first, preferred_element_type=jnp.float32)
    intermediate_activation = (
        jax.nn.silu(projected[:, :hidden_units]) * projected[:, hidden_units:]
    ).astype(jnp.bfloat16)
    result = jnp.dot(intermediate_activation, w_second, preferred_element_type=jnp.float32).astype(
        jnp.bfloat16
    )
    return result.reshape(rows_in.shape)


def shards(tokens, expert_ids, gate_weights, slot_rows, w_in, w_out):
    tok_rows, features = tokens.shape
    experts = slot_rows.shape[1]
    capacity = slot_rows.shape[2]
    w_first = w_in[0]
    w_second = w_out[0]
    own_rows = slot_rows[0]
    token_iota = jnp.arange(tok_rows, dtype=jnp.int32)
    picks = own_rows[:, :, None] == token_iota[None, None, :]
    matches = (
        expert_ids[:, :, None] == jnp.arange(experts, dtype=jnp.int32)[None, None, :]
    ).astype(jnp.float32)
    gate_of = jnp.einsum("tk,tke->et", gate_weights, matches).astype(jnp.bfloat16)
    mixing = jnp.where(picks, gate_of[:, None, :], jnp.zeros((), jnp.bfloat16))
    dispatched = jnp.einsum(
        "ect,td->ecd", picks.astype(jnp.bfloat16), tokens, preferred_element_type=jnp.float32
    ).astype(jnp.bfloat16)
    piece = capacity // CHUNKS
    summed = None
    for k in range(CHUNKS):
        part = dispatched[:, k * piece:(k + 1) * piece]
        arrived = lax.all_to_all(part, "expert", split_axis=0, concat_axis=0, tiled=True)
        response = expert_block(arrived, w_first, w_second)
        returned = lax.all_to_all(response, "expert", split_axis=0, concat_axis=0, tiled=True)
        weights = mixing[:, k * piece:(k + 1) * piece].reshape(-1, tok_rows)
        contrib = jnp.dot(
            weights.T, returned.reshape(-1, features), preferred_element_type=jnp.float32
        )
        summed = contrib if summed is None else summed + contrib
    return summed.astype(jnp.bfloat16)


def solution(mesh):
    in_specs = (
        P(("dp", "expert"), None),
        P(("dp", "expert"), None),
        P(("dp", "expert"), None),
        P(("dp", "expert"), None, None),
        P("expert", None, None),
        P("expert", None, None),
    )
    out_specs = P(("dp", "expert"), None)
    return jax.shard_map(shards, mesh=mesh, in_specs=in_specs, out_specs=out_specs, check_vma=False)
```

```python
import jax
import jax.numpy as jnp
from jax import lax
from jax.sharding import PartitionSpec as P

CHUNKS = 1


def expert_block(rows_in, w_first, w_second):
    features = rows_in.shape[-1]
    hidden_units = w_second.shape[0]
    flat = rows_in.reshape(-1, features)
    projected = jnp.dot(flat, w_first, preferred_element_type=jnp.float32)
    intermediate_activation = (
        jax.nn.silu(projected[:, :hidden_units]) * projected[:, hidden_units:]
    ).astype(jnp.bfloat16)
    result = jnp.dot(intermediate_activation, w_second, preferred_element_type=jnp.float32).astype(
        jnp.bfloat16
    )
    return result.reshape(rows_in.shape)


def shards(tokens, expert_ids, gate_weights, slot_rows, w_in, w_out):
    tok_rows, features = tokens.shape
    experts = slot_rows.shape[1]
    capacity = slot_rows.shape[2]
    w_first = w_in[0]
    w_second = w_out[0]
    own_rows = slot_rows[0]
    token_iota = jnp.arange(tok_rows, dtype=jnp.int32)
    picks = own_rows[:, :, None] == token_iota[None, None, :]
    matches = (
        expert_ids[:, :, None] == jnp.arange(experts, dtype=jnp.int32)[None, None, :]
    ).astype(jnp.float32)
    gate_of = jnp.einsum("tk,tke->et", gate_weights, matches).astype(jnp.bfloat16)
    mixing = jnp.where(picks, gate_of[:, None, :], jnp.zeros((), jnp.bfloat16))
    dispatched = jnp.einsum(
        "ect,td->ecd", picks.astype(jnp.bfloat16), tokens, preferred_element_type=jnp.float32
    ).astype(jnp.bfloat16)
    piece = capacity // CHUNKS
    summed = None
    for k in range(CHUNKS):
        part = dispatched[:, k * piece:(k + 1) * piece]
        arrived = lax.all_to_all(part, "expert", split_axis=0, concat_axis=0, tiled=True)
        response = expert_block(arrived, w_first, w_second)
        returned = lax.all_to_all(response, "expert", split_axis=0, concat_axis=0, tiled=True)
        weights = mixing[:, k * piece:(k + 1) * piece].reshape(-1, tok_rows)
        contrib = jnp.dot(
            weights.T, returned.reshape(-1, features), preferred_element_type=jnp.float32
        )
        summed = contrib if summed is None else summed + contrib
    return summed.astype(jnp.bfloat16)


def solution(mesh):
    in_specs = (
        P(("dp", "expert"), None),
        P(("dp", "expert"), None),
        P(("dp", "expert"), None),
        P(("dp", "expert"), None, None),
        P("expert", None, None),
        P("expert", None, None),
    )
    out_specs = P(("dp", "expert"), None)
    return jax.shard_map(shards, mesh=mesh, in_specs=in_specs, out_specs=out_specs, check_vma=False)
```

```python
import jax
import jax.numpy as jnp
from jax import lax
from jax.sharding import PartitionSpec as P

CHUNKS = 2


def expert_block(rows_in, w_first, w_second):
    features = rows_in.shape[-1]
    hidden_units = w_second.shape[0]
    flat = rows_in.reshape(-1, features)
    projected = jnp.dot(flat, w_first, preferred_element_type=jnp.float32)
    intermediate_activation = (
        jax.nn.silu(projected[:, :hidden_units]) * projected[:, hidden_units:]
    ).astype(jnp.bfloat16)
    result = jnp.dot(intermediate_activation, w_second, preferred_element_type=jnp.float32).astype(
        jnp.bfloat16
    )
    return result.reshape(rows_in.shape)


def shards(tokens, expert_ids, gate_weights, slot_rows, w_in, w_out):
    tok_rows, features = tokens.shape
    experts = slot_rows.shape[1]
    capacity = slot_rows.shape[2]
    w_first = w_in[0]
    w_second = w_out[0]
    own_rows = slot_rows[0]
    token_iota = jnp.arange(tok_rows, dtype=jnp.int32)
    picks = own_rows[:, :, None] == token_iota[None, None, :]
    matches = (
        expert_ids[:, :, None] == jnp.arange(experts, dtype=jnp.int32)[None, None, :]
    ).astype(jnp.float32)
    gate_of = jnp.einsum("tk,tke->et", gate_weights, matches).astype(jnp.bfloat16)
    mixing = jnp.where(picks, gate_of[:, None, :], jnp.zeros((), jnp.bfloat16))
    one_hot = picks.astype(jnp.bfloat16)
    piece = capacity // CHUNKS
    summed = None
    for k in range(CHUNKS):
        part = jnp.einsum(
            "ect,td->ecd",
            one_hot[:, k * piece:(k + 1) * piece],
            tokens,
            preferred_element_type=jnp.float32,
        ).astype(jnp.bfloat16)
        arrived = lax.all_to_all(part, "expert", split_axis=0, concat_axis=0, tiled=True)
        response = expert_block(arrived, w_first, w_second)
        returned = lax.all_to_all(response, "expert", split_axis=0, concat_axis=0, tiled=True)
        weights = mixing[:, k * piece:(k + 1) * piece].reshape(-1, tok_rows)
        contrib = jnp.dot(
            weights.T, returned.reshape(-1, features), preferred_element_type=jnp.float32
        )
        summed = contrib if summed is None else summed + contrib
    return summed.astype(jnp.bfloat16)


def solution(mesh):
    in_specs = (
        P(("dp", "expert"), None),
        P(("dp", "expert"), None),
        P(("dp", "expert"), None),
        P(("dp", "expert"), None, None),
        P("expert", None, None),
        P("expert", None, None),
    )
    out_specs = P(("dp", "expert"), None)
    return jax.shard_map(shards, mesh=mesh, in_specs=in_specs, out_specs=out_specs, check_vma=False)
```

```python
import jax
import jax.numpy as jnp
import numpy as np
from jax import lax
from jax.sharding import Mesh
from jax.sharding import PartitionSpec as P

AXES = ("z", "yh", "core")
RING = 4


def expert_block(rows_in, w_first, w_second):
    features = rows_in.shape[-1]
    hidden_units = w_second.shape[0]
    flat = rows_in.reshape(-1, features)
    projected = jnp.dot(flat, w_first, preferred_element_type=jnp.float32)
    intermediate_activation = (
        jax.nn.silu(projected[:, :hidden_units]) * projected[:, hidden_units:]
    ).astype(jnp.bfloat16)
    result = jnp.dot(intermediate_activation, w_second, preferred_element_type=jnp.float32).astype(
        jnp.bfloat16
    )
    return result.reshape(rows_in.shape)


def shift_z(x, step):
    return lax.ppermute(x, "z", [(i, (i + step) % RING) for i in range(RING)])


def swap(x, axis):
    return lax.ppermute(x, axis, [(0, 1), (1, 0)])


def shards(tokens, expert_ids, gate_weights, slot_rows, w_in, w_out):
    tok_rows, features = tokens.shape
    experts = slot_rows.shape[1]
    capacity = slot_rows.shape[2]
    w_first = w_in[0]
    w_second = w_out[0]
    own_rows = slot_rows[0]
    zi = lax.axis_index("z")
    yi = lax.axis_index("yh")
    ki = lax.axis_index("core")
    n_y = 2
    blocks = RING * n_y

    meta = jnp.zeros((1, features), jnp.bfloat16)
    meta = meta.at[0, : experts * capacity].set(own_rows.reshape(-1).astype(jnp.bfloat16))
    block = jnp.concatenate([tokens, meta], axis=0)

    half = (tok_rows + 1) // 2
    partner = swap(block, "yh")
    from_below = shift_z(block, 1)
    from_above = shift_z(block, -1)
    p_below = shift_z(partner, 1)
    p_above = shift_z(partner, -1)
    far = jnp.concatenate(
        [shift_z(from_below[:half], 1), shift_z(from_above[half:], -1)], axis=0
    )
    p_far = jnp.concatenate([shift_z(p_below[:half], 1), shift_z(p_above[half:], -1)], axis=0)
    rel = jnp.stack([block, partner, from_above, p_above, far, p_far, from_below, p_below])
    toks = rel[:, :tok_rows]
    lists = rel[:, tok_rows, : experts * capacity].astype(jnp.int32).reshape(blocks, experts, capacity)

    chip = zi * n_y + yi
    mine_e = chip * 2 + ki
    pair_e = chip * 2 + (1 - ki)
    sel = jnp.stack(
        [
            lax.dynamic_index_in_dim(lists, mine_e, axis=1, keepdims=False),
            lax.dynamic_index_in_dim(lists, pair_e, axis=1, keepdims=False),
        ],
        axis=1,
    )
    token_iota = jnp.arange(tok_rows, dtype=jnp.int32)
    one_hot = (sel[..., None] == token_iota).astype(jnp.bfloat16)
    disp = jnp.einsum(
        "bjct,btd->bjcd", one_hot, toks, preferred_element_type=jnp.float32
    ).astype(jnp.bfloat16)
    got = swap(disp[:, 1], "core")

    pos = jnp.arange(blocks, dtype=jnp.int32)
    inv = ((pos // n_y - zi) % RING) * n_y + (pos % n_y + yi) % n_y
    out_a = expert_block(disp[:, 0], w_first, w_second)
    a_abs = jnp.take(out_a, inv, axis=0)
    ret_a = lax.all_to_all(a_abs, ("z", "yh"), 0, 0, tiled=True)
    a_abs, got = lax.optimization_barrier((a_abs, got))
    out_b = expert_block(got, w_first, w_second)
    ret_a, out_b = lax.optimization_barrier((ret_a, out_b))
    back_b = swap(out_b, "core")
    b_abs = jnp.take(back_b, inv, axis=0)
    ret_b = lax.all_to_all(b_abs, ("z", "yh"), 0, 0, tiled=True)

    matches = (
        expert_ids[:, :, None] == jnp.arange(experts, dtype=jnp.int32)[None, None, :]
    ).astype(jnp.float32)
    gate_of = jnp.einsum("tk,tke->et", gate_weights, matches).astype(jnp.bfloat16)
    rows3 = own_rows.reshape(blocks, 2, capacity)
    gate3 = gate_of.reshape(blocks, 2, tok_rows)
    summed = None
    for which, returned in ((ki, ret_a), (1 - ki, ret_b)):
        rows = lax.dynamic_index_in_dim(rows3, which, axis=1, keepdims=False)
        gates = lax.dynamic_index_in_dim(gate3, which, axis=1, keepdims=False)
        mixing = jnp.where(
            rows[:, :, None] == token_iota[None, None, :],
            gates[:, None, :],
            jnp.zeros((), jnp.bfloat16),
        )
        contrib = jnp.dot(
            mixing.reshape(-1, tok_rows).T,
            returned.reshape(-1, features),
            preferred_element_type=jnp.float32,
        )
        summed = contrib if summed is None else summed + contrib
    return summed.astype(jnp.bfloat16)


def solution(mesh):
    devices = np.asarray(mesh.devices)
    groups = devices.shape[0]
    fine = Mesh(devices.reshape(groups, RING, 2, 2), ("dp",) + AXES)
    rows = ("dp",) + AXES
    in_specs = (
        P(rows, None),
        P(rows, None),
        P(rows, None),
        P(rows, None, None),
        P(AXES, None, None),
        P(AXES, None, None),
    )
    out_specs = P(rows, None)
    return jax.shard_map(shards, mesh=fine, in_specs=in_specs, out_specs=out_specs, check_vma=False)
```

```python
import jax
import jax.numpy as jnp
import numpy as np
from jax import lax
from jax.sharding import Mesh
from jax.sharding import PartitionSpec as P

AXES = ("z", "yh", "core")
RING = 4


def expert_block(rows_in, w_first, w_second):
    features = rows_in.shape[-1]
    hidden_units = w_second.shape[0]
    flat = rows_in.reshape(-1, features)
    projected = jnp.dot(flat, w_first, preferred_element_type=jnp.float32)
    intermediate_activation = (
        jax.nn.silu(projected[:, :hidden_units]) * projected[:, hidden_units:]
    ).astype(jnp.bfloat16)
    result = jnp.dot(intermediate_activation, w_second, preferred_element_type=jnp.float32).astype(
        jnp.bfloat16
    )
    return result.reshape(rows_in.shape)


def shift_z(x, step):
    return lax.ppermute(x, "z", [(i, (i + step) % RING) for i in range(RING)])


def swap(x, axis):
    return lax.ppermute(x, axis, [(0, 1), (1, 0)])


def shards(tokens, expert_ids, gate_weights, slot_rows, w_in, w_out):
    tok_rows, features = tokens.shape
    experts = slot_rows.shape[1]
    capacity = slot_rows.shape[2]
    w_first = w_in[0]
    w_second = w_out[0]
    own_rows = slot_rows[0]
    zi = lax.axis_index("z")
    yi = lax.axis_index("yh")
    ki = lax.axis_index("core")
    n_y = 2
    blocks = RING * n_y

    meta = jnp.zeros((1, features), jnp.bfloat16)
    meta = meta.at[0, : experts * capacity].set(own_rows.reshape(-1).astype(jnp.bfloat16))
    block = jnp.concatenate([tokens, meta], axis=0)

    half = (tok_rows + 1) // 2
    partner = swap(block, "yh")
    from_below = shift_z(block, 1)
    from_above = shift_z(block, -1)
    p_below = shift_z(partner, 1)
    p_above = shift_z(partner, -1)
    far = jnp.concatenate(
        [shift_z(from_below[:half], 1), shift_z(from_above[half:], -1)], axis=0
    )
    p_far = jnp.concatenate([shift_z(p_below[:half], 1), shift_z(p_above[half:], -1)], axis=0)

    chip = zi * n_y + yi
    mine_e = chip * 2 + ki
    pair_e = chip * 2 + (1 - ki)
    token_iota = jnp.arange(tok_rows, dtype=jnp.int32)

    def slots_of(pieces):
        stacked = jnp.stack([arr for _, _, arr in pieces])
        toks = stacked[:, :tok_rows]
        lists = stacked[:, tok_rows, : experts * capacity].astype(jnp.int32)
        lists = lists.reshape(len(pieces), experts, capacity)
        sel = jnp.stack(
            [
                lax.dynamic_index_in_dim(lists, mine_e, axis=1, keepdims=False),
                lax.dynamic_index_in_dim(lists, pair_e, axis=1, keepdims=False),
            ],
            axis=1,
        )
        one_hot = (sel[..., None] == token_iota).astype(jnp.bfloat16)
        disp = jnp.einsum(
            "bjct,btd->bjcd", one_hot, toks, preferred_element_type=jnp.float32
        ).astype(jnp.bfloat16)
        return disp[:, 0], swap(disp[:, 1], "core")

    def place(into, pieces, outs):
        for i, (r, q, _) in enumerate(pieces):
            where = ((zi + r) % RING) * n_y + (yi + q) % n_y
            into = lax.dynamic_update_slice(into, outs[i : i + 1], (where, 0, 0))
        return into

    early = [(0, 0, block), (0, 1, partner), (1, 0, from_above), (3, 0, from_below)]
    late = [(2, 0, far), (2, 1, p_far), (1, 1, p_above), (3, 1, p_below)]
    mine_1, got_1 = slots_of(early)
    out_m1 = expert_block(mine_1, w_first, w_second)
    out_g1 = expert_block(got_1, w_first, w_second)
    late_arrs = [arr for _, _, arr in late]
    *late_arrs, out_m1, out_g1 = lax.optimization_barrier((*late_arrs, out_m1, out_g1))
    late = [(r, q, arr) for (r, q, _), arr in zip(late, late_arrs)]
    mine_2, got_2 = slots_of(late)
    out_m2 = expert_block(mine_2, w_first, w_second)
    empty = jnp.zeros((blocks, capacity, features), jnp.bfloat16)
    a_abs = place(place(empty, early, out_m1), late, out_m2)
    ret_a = lax.all_to_all(a_abs, ("z", "yh"), 0, 0, tiled=True)
    a_abs, got_2 = lax.optimization_barrier((a_abs, got_2))
    out_g2 = expert_block(got_2, w_first, w_second)
    b_abs = place(place(empty, early, swap(out_g1, "core")), late, swap(out_g2, "core"))
    ret_a, b_abs = lax.optimization_barrier((ret_a, b_abs))
    ret_b = lax.all_to_all(b_abs, ("z", "yh"), 0, 0, tiled=True)

    matches = (
        expert_ids[:, :, None] == jnp.arange(experts, dtype=jnp.int32)[None, None, :]
    ).astype(jnp.float32)
    gate_of = jnp.einsum("tk,tke->et", gate_weights, matches).astype(jnp.bfloat16)
    rows3 = own_rows.reshape(blocks, 2, capacity)
    gate3 = gate_of.reshape(blocks, 2, tok_rows)
    summed = None
    for which, returned in ((ki, ret_a), (1 - ki, ret_b)):
        rows = lax.dynamic_index_in_dim(rows3, which, axis=1, keepdims=False)
        gates = lax.dynamic_index_in_dim(gate3, which, axis=1, keepdims=False)
        mixing = jnp.where(
            rows[:, :, None] == token_iota[None, None, :],
            gates[:, None, :],
            jnp.zeros((), jnp.bfloat16),
        )
        contrib = jnp.dot(
            mixing.reshape(-1, tok_rows).T,
            returned.reshape(-1, features),
            preferred_element_type=jnp.float32,
        )
        summed = contrib if summed is None else summed + contrib
    return summed.astype(jnp.bfloat16)


def solution(mesh):
    devices = np.asarray(mesh.devices)
    groups = devices.shape[0]
    fine = Mesh(devices.reshape(groups, RING, 2, 2), ("dp",) + AXES)
    rows = ("dp",) + AXES
    in_specs = (
        P(rows, None),
        P(rows, None),
        P(rows, None),
        P(rows, None, None),
        P(AXES, None, None),
        P(AXES, None, None),
    )
    out_specs = P(rows, None)
    return jax.shard_map(shards, mesh=fine, in_specs=in_specs, out_specs=out_specs, check_vma=False)
```

```python
import jax
import jax.numpy as jnp
import numpy as np
from jax import lax
from jax.sharding import Mesh
from jax.sharding import PartitionSpec as P

AXES = ("z", "yh", "core")
RING = 4


def expert_block(rows_in, w_first, w_second):
    features = rows_in.shape[-1]
    hidden_units = w_second.shape[0]
    flat = rows_in.reshape(-1, features)
    projected = jnp.dot(flat, w_first, preferred_element_type=jnp.float32)
    intermediate_activation = (
        jax.nn.silu(projected[:, :hidden_units]) * projected[:, hidden_units:]
    ).astype(jnp.bfloat16)
    result = jnp.dot(intermediate_activation, w_second, preferred_element_type=jnp.float32).astype(
        jnp.bfloat16
    )
    return result.reshape(rows_in.shape)


def shift_z(x, step):
    return lax.ppermute(x, "z", [(i, (i + step) % RING) for i in range(RING)])


def swap(x, axis):
    return lax.ppermute(x, axis, [(0, 1), (1, 0)])


def shards(tokens, expert_ids, gate_weights, slot_rows, w_in, w_out):
    tok_rows, features = tokens.shape
    experts = slot_rows.shape[1]
    capacity = slot_rows.shape[2]
    w_first = w_in[0]
    w_second = w_out[0]
    own_rows = slot_rows[0]
    zi = lax.axis_index("z")
    yi = lax.axis_index("yh")
    ki = lax.axis_index("core")
    n_y = 2
    blocks = RING * n_y

    meta = jnp.zeros((1, features), jnp.bfloat16)
    meta = meta.at[0, : experts * capacity].set(own_rows.reshape(-1).astype(jnp.bfloat16))
    block = jnp.concatenate([tokens, meta], axis=0)

    half = (tok_rows + 1) // 2
    partner = swap(block, "yh")
    from_below = shift_z(block, 1)
    from_above = shift_z(block, -1)
    p_below = shift_z(partner, 1)
    p_above = shift_z(partner, -1)
    far = jnp.concatenate(
        [shift_z(from_below[:half], 1), shift_z(from_above[half:], -1)], axis=0
    )
    p_far = jnp.concatenate([shift_z(p_below[:half], 1), shift_z(p_above[half:], -1)], axis=0)

    chip = zi * n_y + yi
    mine_e = chip * 2 + ki
    pair_e = chip * 2 + (1 - ki)
    token_iota = jnp.arange(tok_rows, dtype=jnp.int32)

    def slots_of(pieces):
        stacked = jnp.stack([arr for _, _, arr in pieces])
        toks = stacked[:, :tok_rows]
        lists = stacked[:, tok_rows, : experts * capacity].astype(jnp.int32)
        lists = lists.reshape(len(pieces), experts, capacity)
        sel = jnp.stack(
            [
                lax.dynamic_index_in_dim(lists, mine_e, axis=1, keepdims=False),
                lax.dynamic_index_in_dim(lists, pair_e, axis=1, keepdims=False),
            ],
            axis=1,
        )
        one_hot = (sel[..., None] == token_iota).astype(jnp.bfloat16)
        disp = jnp.einsum(
            "bjct,btd->bjcd", one_hot, toks, preferred_element_type=jnp.float32
        ).astype(jnp.bfloat16)
        return disp[:, 0], swap(disp[:, 1], "core")

    def place(into, pieces, outs):
        for i, (r, q, _) in enumerate(pieces):
            where = ((zi + r) % RING) * n_y + (yi + q) % n_y
            into = lax.dynamic_update_slice(into, outs[i : i + 1], (where, 0, 0))
        return into

    early = [(0, 0, block), (0, 1, partner), (1, 0, from_above), (3, 0, from_below)]
    late = [(2, 0, far), (2, 1, p_far), (1, 1, p_above), (3, 1, p_below)]
    mine_1, got_1 = slots_of(early)
    out_m1 = expert_block(mine_1, w_first, w_second)
    out_g1 = expert_block(got_1, w_first, w_second)
    empty = jnp.zeros((blocks, capacity, features), jnp.bfloat16)
    a_part = place(empty, early, out_m1)
    late_arrs = [arr for _, _, arr in late]
    *late_arrs, a_part = lax.optimization_barrier((*late_arrs, a_part))
    late = [(r, q, arr) for (r, q, _), arr in zip(late, late_arrs)]
    mine_2, got_2 = slots_of(late)
    out_m2 = expert_block(mine_2, w_first, w_second)
    a_abs = place(a_part, late, out_m2)
    ret_a = lax.all_to_all(a_abs, ("z", "yh"), 0, 0, tiled=True)
    a_abs, got_2 = lax.optimization_barrier((a_abs, got_2))
    out_g2 = expert_block(got_2, w_first, w_second)
    b_abs = place(place(empty, early, swap(out_g1, "core")), late, swap(out_g2, "core"))
    ret_a, b_abs = lax.optimization_barrier((ret_a, b_abs))
    ret_b = lax.all_to_all(b_abs, ("z", "yh"), 0, 0, tiled=True)

    matches = (
        expert_ids[:, :, None] == jnp.arange(experts, dtype=jnp.int32)[None, None, :]
    ).astype(jnp.float32)
    gate_of = jnp.einsum("tk,tke->et", gate_weights, matches).astype(jnp.bfloat16)
    rows3 = own_rows.reshape(blocks, 2, capacity)
    gate3 = gate_of.reshape(blocks, 2, tok_rows)

    def contribution(which, returned):
        rows = lax.dynamic_index_in_dim(rows3, which, axis=1, keepdims=False)
        gates = lax.dynamic_index_in_dim(gate3, which, axis=1, keepdims=False)
        mixing = jnp.where(
            rows[:, :, None] == token_iota[None, None, :],
            gates[:, None, :],
            jnp.zeros((), jnp.bfloat16),
        )
        return jnp.dot(
            mixing.reshape(-1, tok_rows).T,
            returned.reshape(-1, features),
            preferred_element_type=jnp.float32,
        )

    first = contribution(ki, ret_a)
    ret_b, first = lax.optimization_barrier((ret_b, first))
    summed = first + contribution(1 - ki, ret_b)
    return summed.astype(jnp.bfloat16)


def solution(mesh):
    devices = np.asarray(mesh.devices)
    groups = devices.shape[0]
    fine = Mesh(devices.reshape(groups, RING, 2, 2), ("dp",) + AXES)
    rows = ("dp",) + AXES
    in_specs = (
        P(rows, None),
        P(rows, None),
        P(rows, None),
        P(rows, None, None),
        P(AXES, None, None),
        P(AXES, None, None),
    )
    out_specs = P(rows, None)
    return jax.shard_map(shards, mesh=fine, in_specs=in_specs, out_specs=out_specs, check_vma=False)
```

```python
import jax
import jax.numpy as jnp
import numpy as np
from jax import lax
from jax.sharding import Mesh
from jax.sharding import PartitionSpec as P

AXES = ("z", "yh", "core")
RING = 4


def expert_block(rows_in, w_first, w_second):
    features = rows_in.shape[-1]
    hidden_units = w_second.shape[0]
    flat = rows_in.reshape(-1, features)
    projected = jnp.dot(flat, w_first, preferred_element_type=jnp.float32)
    intermediate_activation = (
        jax.nn.silu(projected[:, :hidden_units]) * projected[:, hidden_units:]
    ).astype(jnp.bfloat16)
    result = jnp.dot(intermediate_activation, w_second, preferred_element_type=jnp.float32).astype(
        jnp.bfloat16
    )
    return result.reshape(rows_in.shape)


def shift_z(x, step):
    return lax.ppermute(x, "z", [(i, (i + step) % RING) for i in range(RING)])


def swap(x, axis):
    return lax.ppermute(x, axis, [(0, 1), (1, 0)])


def shards(tokens, expert_ids, gate_weights, slot_rows, w_in, w_out):
    tok_rows, features = tokens.shape
    experts = slot_rows.shape[1]
    capacity = slot_rows.shape[2]
    w_first = w_in[0]
    w_second = w_out[0]
    own_rows = slot_rows[0]
    zi = lax.axis_index("z")
    yi = lax.axis_index("yh")
    ki = lax.axis_index("core")
    n_y = 2
    blocks = RING * n_y

    meta = jnp.zeros((1, features), jnp.bfloat16)
    meta = meta.at[0, : experts * capacity].set(own_rows.reshape(-1).astype(jnp.bfloat16))
    block = jnp.concatenate([tokens, meta], axis=0)

    half = (tok_rows + 1) // 2
    partner = swap(block, "yh")
    from_below = shift_z(block, 1)
    from_above = shift_z(block, -1)
    p_below = shift_z(partner, 1)
    p_above = shift_z(partner, -1)
    far = jnp.concatenate(
        [shift_z(from_below[:half], 1), shift_z(from_above[half:], -1)], axis=0
    )
    p_far = jnp.concatenate([shift_z(p_below[:half], 1), shift_z(p_above[half:], -1)], axis=0)

    chip = zi * n_y + yi
    mine_e = chip * 2 + ki
    pair_e = chip * 2 + (1 - ki)
    token_iota = jnp.arange(tok_rows, dtype=jnp.int32)

    def slots_of(pieces):
        stacked = jnp.stack([arr for _, _, arr in pieces])
        toks = stacked[:, :tok_rows]
        lists = stacked[:, tok_rows, : experts * capacity].astype(jnp.int32)
        lists = lists.reshape(len(pieces), experts, capacity)
        sel = jnp.stack(
            [
                lax.dynamic_index_in_dim(lists, mine_e, axis=1, keepdims=False),
                lax.dynamic_index_in_dim(lists, pair_e, axis=1, keepdims=False),
            ],
            axis=1,
        )
        one_hot = (sel[..., None] == token_iota).astype(jnp.bfloat16)
        disp = jnp.einsum(
            "bjct,btd->bjcd", one_hot, toks, preferred_element_type=jnp.float32
        ).astype(jnp.bfloat16)
        return disp[:, 0], swap(disp[:, 1], "core")

    def place(into, pieces, outs):
        for i, (r, q, _) in enumerate(pieces):
            where = ((zi + r) % RING) * n_y + (yi + q) % n_y
            into = lax.dynamic_update_slice(into, outs[i : i + 1], (where, 0, 0))
        return into

    stages = [
        [(0, 0, block), (0, 1, partner), (1, 0, from_above), (3, 0, from_below)],
        [(2, 0, far), (1, 1, p_above), (3, 1, p_below)],
        [(2, 1, p_far)],
    ]
    a_abs = jnp.zeros((blocks, capacity, features), jnp.bfloat16)
    got_outs = []
    for n, pieces in enumerate(stages):
        if n:
            arrs = [arr for _, _, arr in pieces]
            *arrs, a_abs = lax.optimization_barrier((*arrs, a_abs))
            pieces = [(r, q, arr) for (r, q, _), arr in zip(pieces, arrs)]
            stages[n] = pieces
        mine, got = slots_of(pieces)
        a_abs = place(a_abs, pieces, expert_block(mine, w_first, w_second))
        got_outs.append(got)
    ret_a = lax.all_to_all(a_abs, ("z", "yh"), 0, 0, tiled=True)
    a_abs, *got_outs = lax.optimization_barrier((a_abs, *got_outs))
    b_abs = jnp.zeros((blocks, capacity, features), jnp.bfloat16)
    for pieces, got in zip(stages, got_outs):
        b_abs = place(b_abs, pieces, swap(expert_block(got, w_first, w_second), "core"))
    ret_a, b_abs = lax.optimization_barrier((ret_a, b_abs))
    ret_b = lax.all_to_all(b_abs, ("z", "yh"), 0, 0, tiled=True)

    matches = (
        expert_ids[:, :, None] == jnp.arange(experts, dtype=jnp.int32)[None, None, :]
    ).astype(jnp.float32)
    gate_of = jnp.einsum("tk,tke->et", gate_weights, matches).astype(jnp.bfloat16)
    rows3 = own_rows.reshape(blocks, 2, capacity)
    gate3 = gate_of.reshape(blocks, 2, tok_rows)

    def contribution(which, returned):
        rows = lax.dynamic_index_in_dim(rows3, which, axis=1, keepdims=False)
        gates = lax.dynamic_index_in_dim(gate3, which, axis=1, keepdims=False)
        mixing = jnp.where(
            rows[:, :, None] == token_iota[None, None, :],
            gates[:, None, :],
            jnp.zeros((), jnp.bfloat16),
        )
        return jnp.dot(
            mixing.reshape(-1, tok_rows).T,
            returned.reshape(-1, features),
            preferred_element_type=jnp.float32,
        )

    first = contribution(ki, ret_a)
    ret_b, first = lax.optimization_barrier((ret_b, first))
    summed = first + contribution(1 - ki, ret_b)
    return summed.astype(jnp.bfloat16)


def solution(mesh):
    devices = np.asarray(mesh.devices)
    groups = devices.shape[0]
    fine = Mesh(devices.reshape(groups, RING, 2, 2), ("dp",) + AXES)
    rows = ("dp",) + AXES
    in_specs = (
        P(rows, None),
        P(rows, None),
        P(rows, None),
        P(rows, None, None),
        P(AXES, None, None),
        P(AXES, None, None),
    )
    out_specs = P(rows, None)
    return jax.shard_map(shards, mesh=fine, in_specs=in_specs, out_specs=out_specs, check_vma=False)
```

```python
import jax
import jax.numpy as jnp
from jax import lax
from jax.sharding import PartitionSpec as P

CHUNKS = 2


def expert_block(rows_in, w_first, w_second):
    features = rows_in.shape[-1]
    hidden_units = w_second.shape[0]
    flat = rows_in.reshape(-1, features)
    projected = jnp.dot(flat, w_first, preferred_element_type=jnp.float32)
    intermediate_activation = (
        jax.nn.silu(projected[:, :hidden_units]) * projected[:, hidden_units:]
    ).astype(jnp.bfloat16)
    result = jnp.dot(intermediate_activation, w_second, preferred_element_type=jnp.float32).astype(
        jnp.bfloat16
    )
    return result.reshape(rows_in.shape)


def shards(tokens, expert_ids, gate_weights, slot_rows, w_in, w_out):
    tok_rows, features = tokens.shape
    experts = slot_rows.shape[1]
    capacity = slot_rows.shape[2]
    w_first = w_in[0]
    w_second = w_out[0]
    own_rows = slot_rows[0]
    token_iota = jnp.arange(tok_rows, dtype=jnp.int32)
    picks = own_rows[:, :, None] == token_iota[None, None, :]
    matches = (
        expert_ids[:, :, None] == jnp.arange(experts, dtype=jnp.int32)[None, None, :]
    ).astype(jnp.float32)
    gate_of = jnp.einsum("tk,tke->et", gate_weights, matches).astype(jnp.bfloat16)
    mixing = jnp.where(picks, gate_of[:, None, :], jnp.zeros((), jnp.bfloat16))
    one_hot = picks.astype(jnp.bfloat16)
    piece = capacity // CHUNKS
    me = lax.axis_index("expert")
    summed = None
    for k in range(CHUNKS):
        part = jnp.einsum(
            "ect,td->ecd",
            one_hot[:, k * piece:(k + 1) * piece],
            tokens,
            preferred_element_type=jnp.float32,
        ).astype(jnp.bfloat16)
        arrived = lax.all_to_all(part, "expert", split_axis=0, concat_axis=0, tiled=True)
        response = expert_block(arrived, w_first, w_second)
        weights = mixing[:, k * piece:(k + 1) * piece]
        if k == 0:
            contrib = None
            for shift in range(experts):
                sent = lax.dynamic_index_in_dim(response, (me + shift) % experts, 0, keepdims=False)
                if shift:
                    perm = [(i, (i + shift) % experts) for i in range(experts)]
                    sent = lax.ppermute(sent, "expert", perm)
                w = lax.dynamic_index_in_dim(weights, (me - shift) % experts, 0, keepdims=False)
                c = jnp.dot(w.T, sent, preferred_element_type=jnp.float32)
                contrib = c if contrib is None else contrib + c
        else:
            returned = lax.all_to_all(response, "expert", split_axis=0, concat_axis=0, tiled=True)
            contrib = jnp.dot(
                weights.reshape(-1, tok_rows).T,
                returned.reshape(-1, features),
                preferred_element_type=jnp.float32,
            )
        summed = contrib if summed is None else summed + contrib
    return summed.astype(jnp.bfloat16)


def solution(mesh):
    in_specs = (
        P(("dp", "expert"), None),
        P(("dp", "expert"), None),
        P(("dp", "expert"), None),
        P(("dp", "expert"), None, None),
        P("expert", None, None),
        P("expert", None, None),
    )
    out_specs = P(("dp", "expert"), None)
    return jax.shard_map(shards, mesh=mesh, in_specs=in_specs, out_specs=out_specs, check_vma=False)
```

```python
import jax
import jax.numpy as jnp
import numpy as np
from jax import lax
from jax.sharding import Mesh
from jax.sharding import PartitionSpec as P

AXES = ("z", "yh", "core")
RING = 4


def expert_block(rows_in, w_first, w_second):
    features = rows_in.shape[-1]
    hidden_units = w_second.shape[0]
    flat = rows_in.reshape(-1, features)
    projected = jnp.dot(flat, w_first, preferred_element_type=jnp.float32)
    intermediate_activation = (
        jax.nn.silu(projected[:, :hidden_units]) * projected[:, hidden_units:]
    ).astype(jnp.bfloat16)
    result = jnp.dot(intermediate_activation, w_second, preferred_element_type=jnp.float32).astype(
        jnp.bfloat16
    )
    return result.reshape(rows_in.shape)


def shift_z(x, step):
    return lax.ppermute(x, "z", [(i, (i + step) % RING) for i in range(RING)])


def swap(x, axis):
    return lax.ppermute(x, axis, [(0, 1), (1, 0)])


def shards(tokens, expert_ids, gate_weights, slot_rows, w_in, w_out):
    tok_rows, features = tokens.shape
    experts = slot_rows.shape[1]
    capacity = slot_rows.shape[2]
    w_first = w_in[0]
    w_second = w_out[0]
    own_rows = slot_rows[0]
    zi = lax.axis_index("z")
    yi = lax.axis_index("yh")
    ki = lax.axis_index("core")
    n_y = 2
    blocks = RING * n_y

    meta = jnp.zeros((1, features), jnp.bfloat16)
    meta = meta.at[0, : experts * capacity].set(own_rows.reshape(-1).astype(jnp.bfloat16))
    block = jnp.concatenate([tokens, meta], axis=0)

    half = (tok_rows + 1) // 2
    partner = swap(block, "yh")
    from_below = shift_z(block, 1)
    from_above = shift_z(block, -1)
    rows = tok_rows + 1
    up = shift_z(jnp.concatenate([partner, from_below[:half]], axis=0), 1)
    down = shift_z(jnp.concatenate([partner, from_above[half:]], axis=0), -1)
    p_below = up[:rows]
    p_above = down[:rows]
    far = jnp.concatenate([up[rows:], down[rows:]], axis=0)
    p_far = jnp.concatenate([shift_z(p_below[:half], 1), shift_z(p_above[half:], -1)], axis=0)

    chip = zi * n_y + yi
    mine_e = chip * 2 + ki
    pair_e = chip * 2 + (1 - ki)
    token_iota = jnp.arange(tok_rows, dtype=jnp.int32)

    def slots_of(pieces):
        stacked = jnp.stack([arr for _, _, arr in pieces])
        toks = stacked[:, :tok_rows]
        lists = stacked[:, tok_rows, : experts * capacity].astype(jnp.int32)
        lists = lists.reshape(len(pieces), experts, capacity)
        sel = jnp.stack(
            [
                lax.dynamic_index_in_dim(lists, mine_e, axis=1, keepdims=False),
                lax.dynamic_index_in_dim(lists, pair_e, axis=1, keepdims=False),
            ],
            axis=1,
        )
        one_hot = (sel[..., None] == token_iota).astype(jnp.bfloat16)
        disp = jnp.einsum(
            "bjct,btd->bjcd", one_hot, toks, preferred_element_type=jnp.float32
        ).astype(jnp.bfloat16)
        return disp[:, 0], swap(disp[:, 1], "core")

    def place(into, pieces, outs):
        for i, (r, q, _) in enumerate(pieces):
            where = ((zi + r) % RING) * n_y + (yi + q) % n_y
            into = lax.dynamic_update_slice(into, outs[i : i + 1], (where, 0, 0))
        return into

    early = [(0, 0, block), (0, 1, partner), (1, 0, from_above), (3, 0, from_below)]
    late = [(2, 0, far), (2, 1, p_far), (1, 1, p_above), (3, 1, p_below)]
    mine_1, got_1 = slots_of(early)
    out_m1 = expert_block(mine_1, w_first, w_second)
    out_g1 = expert_block(got_1, w_first, w_second)
    empty = jnp.zeros((blocks, capacity, features), jnp.bfloat16)
    a_part = place(empty, early, out_m1)
    late_arrs = [arr for _, _, arr in late]
    *late_arrs, a_part = lax.optimization_barrier((*late_arrs, a_part))
    late = [(r, q, arr) for (r, q, _), arr in zip(late, late_arrs)]
    mine_2, got_2 = slots_of(late)
    out_m2 = expert_block(mine_2, w_first, w_second)
    a_abs = place(a_part, late, out_m2)
    ret_a = lax.all_to_all(a_abs, ("z", "yh"), 0, 0, tiled=True)
    a_abs, got_2 = lax.optimization_barrier((a_abs, got_2))
    out_g2 = expert_block(got_2, w_first, w_second)
    b_abs = place(place(empty, early, swap(out_g1, "core")), late, swap(out_g2, "core"))
    ret_a, b_abs = lax.optimization_barrier((ret_a, b_abs))
    ret_b = lax.all_to_all(b_abs, ("z", "yh"), 0, 0, tiled=True)

    matches = (
        expert_ids[:, :, None] == jnp.arange(experts, dtype=jnp.int32)[None, None, :]
    ).astype(jnp.float32)
    gate_of = jnp.einsum("tk,tke->et", gate_weights, matches).astype(jnp.bfloat16)
    rows3 = own_rows.reshape(blocks, 2, capacity)
    gate3 = gate_of.reshape(blocks, 2, tok_rows)

    def contribution(which, returned):
        rows = lax.dynamic_index_in_dim(rows3, which, axis=1, keepdims=False)
        gates = lax.dynamic_index_in_dim(gate3, which, axis=1, keepdims=False)
        mixing = jnp.where(
            rows[:, :, None] == token_iota[None, None, :],
            gates[:, None, :],
            jnp.zeros((), jnp.bfloat16),
        )
        return jnp.dot(
            mixing.reshape(-1, tok_rows).T,
            returned.reshape(-1, features),
            preferred_element_type=jnp.float32,
        )

    first = contribution(ki, ret_a)
    ret_b, first = lax.optimization_barrier((ret_b, first))
    summed = first + contribution(1 - ki, ret_b)
    return summed.astype(jnp.bfloat16)


def solution(mesh):
    devices = np.asarray(mesh.devices)
    groups = devices.shape[0]
    fine = Mesh(devices.reshape(groups, RING, 2, 2), ("dp",) + AXES)
    rows = ("dp",) + AXES
    in_specs = (
        P(rows, None),
        P(rows, None),
        P(rows, None),
        P(rows, None, None),
        P(AXES, None, None),
        P(AXES, None, None),
    )
    out_specs = P(rows, None)
    return jax.shard_map(shards, mesh=fine, in_specs=in_specs, out_specs=out_specs, check_vma=False)
```

```python
import jax
import jax.numpy as jnp
import numpy as np
from jax import lax
from jax.sharding import Mesh
from jax.sharding import PartitionSpec as P

AXES = ("z", "yh", "core")
RING = 4


def expert_block(rows_in, w_first, w_second):
    features = rows_in.shape[-1]
    hidden_units = w_second.shape[0]
    flat = rows_in.reshape(-1, features)
    projected = jnp.dot(flat, w_first, preferred_element_type=jnp.float32)
    intermediate_activation = (
        jax.nn.silu(projected[:, :hidden_units]) * projected[:, hidden_units:]
    ).astype(jnp.bfloat16)
    result = jnp.dot(intermediate_activation, w_second, preferred_element_type=jnp.float32).astype(
        jnp.bfloat16
    )
    return result.reshape(rows_in.shape)


def shift_z(x, step):
    return lax.ppermute(x, "z", [(i, (i + step) % RING) for i in range(RING)])


def swap(x, axis):
    return lax.ppermute(x, axis, [(0, 1), (1, 0)])


def shards(tokens, expert_ids, gate_weights, slot_rows, w_in, w_out):
    tok_rows, features = tokens.shape
    experts = slot_rows.shape[1]
    capacity = slot_rows.shape[2]
    w_first = w_in[0]
    w_second = w_out[0]
    own_rows = slot_rows[0]
    zi = lax.axis_index("z")
    yi = lax.axis_index("yh")
    ki = lax.axis_index("core")
    n_y = 2
    blocks = RING * n_y

    meta = jnp.zeros((1, features), jnp.bfloat16)
    meta = meta.at[0, : experts * capacity].set(own_rows.reshape(-1).astype(jnp.bfloat16))
    block = jnp.concatenate([tokens, meta], axis=0)

    half = (tok_rows + 1) // 2
    partner = swap(block, "yh")
    from_below = shift_z(block, 1)
    from_above = shift_z(block, -1)
    rows = tok_rows + 1
    up = shift_z(jnp.concatenate([partner, from_below[:half]], axis=0), 1)
    down = shift_z(jnp.concatenate([partner, from_above[half:]], axis=0), -1)
    p_below = up[:rows]
    p_above = down[:rows]
    far = jnp.concatenate([up[rows:], down[rows:]], axis=0)
    p_far = jnp.concatenate([shift_z(p_below[:half], 1), shift_z(p_above[half:], -1)], axis=0)

    chip = zi * n_y + yi
    mine_e = chip * 2 + ki
    pair_e = chip * 2 + (1 - ki)
    token_iota = jnp.arange(tok_rows, dtype=jnp.int32)

    def slots_of(pieces):
        stacked = jnp.stack([arr for _, _, arr in pieces])
        toks = stacked[:, :tok_rows]
        lists = stacked[:, tok_rows, : experts * capacity].astype(jnp.int32)
        lists = lists.reshape(len(pieces), experts, capacity)
        sel = jnp.stack(
            [
                lax.dynamic_index_in_dim(lists, mine_e, axis=1, keepdims=False),
                lax.dynamic_index_in_dim(lists, pair_e, axis=1, keepdims=False),
            ],
            axis=1,
        )
        one_hot = (sel[..., None] == token_iota).astype(jnp.bfloat16)
        disp = jnp.einsum(
            "bjct,btd->bjcd", one_hot, toks, preferred_element_type=jnp.float32
        ).astype(jnp.bfloat16)
        return disp[:, 0], swap(disp[:, 1], "core")

    def place(into, pieces, outs):
        for i, (r, q, _) in enumerate(pieces):
            where = ((zi + r) % RING) * n_y + (yi + q) % n_y
            into = lax.dynamic_update_slice(into, outs[i : i + 1], (where, 0, 0))
        return into

    early = [(0, 0, block), (0, 1, partner), (1, 0, from_above), (3, 0, from_below)]
    late = [(2, 0, far), (2, 1, p_far), (1, 1, p_above), (3, 1, p_below)]
    mine_1, got_1 = slots_of(early)
    out_m1 = expert_block(mine_1, w_first, w_second)
    empty = jnp.zeros((blocks, capacity, features), jnp.bfloat16)
    a_part = place(empty, early, out_m1)
    late_arrs = [arr for _, _, arr in late]
    *late_arrs, a_part = lax.optimization_barrier((*late_arrs, a_part))
    late = [(r, q, arr) for (r, q, _), arr in zip(late, late_arrs)]
    mine_2, got_2 = slots_of(late)
    out_m2 = expert_block(mine_2, w_first, w_second)
    a_abs = place(a_part, late, out_m2)
    ret_a = lax.all_to_all(a_abs, ("z", "yh"), 0, 0, tiled=True)
    a_abs, got_1, got_2 = lax.optimization_barrier((a_abs, got_1, got_2))
    out_g1 = expert_block(got_1, w_first, w_second)
    out_g2 = expert_block(got_2, w_first, w_second)
    b_abs = place(place(empty, early, swap(out_g1, "core")), late, swap(out_g2, "core"))
    ret_a, b_abs = lax.optimization_barrier((ret_a, b_abs))
    ret_b = lax.all_to_all(b_abs, ("z", "yh"), 0, 0, tiled=True)

    matches = (
        expert_ids[:, :, None] == jnp.arange(experts, dtype=jnp.int32)[None, None, :]
    ).astype(jnp.float32)
    gate_of = jnp.einsum("tk,tke->et", gate_weights, matches).astype(jnp.bfloat16)
    rows3 = own_rows.reshape(blocks, 2, capacity)
    gate3 = gate_of.reshape(blocks, 2, tok_rows)

    def contribution(which, returned):
        rows = lax.dynamic_index_in_dim(rows3, which, axis=1, keepdims=False)
        gates = lax.dynamic_index_in_dim(gate3, which, axis=1, keepdims=False)
        mixing = jnp.where(
            rows[:, :, None] == token_iota[None, None, :],
            gates[:, None, :],
            jnp.zeros((), jnp.bfloat16),
        )
        return jnp.dot(
            mixing.reshape(-1, tok_rows).T,
            returned.reshape(-1, features),
            preferred_element_type=jnp.float32,
        )

    first = contribution(ki, ret_a)
    ret_b, first = lax.optimization_barrier((ret_b, first))
    summed = first + contribution(1 - ki, ret_b)
    return summed.astype(jnp.bfloat16)


def solution(mesh):
    devices = np.asarray(mesh.devices)
    groups = devices.shape[0]
    fine = Mesh(devices.reshape(groups, RING, 2, 2), ("dp",) + AXES)
    rows = ("dp",) + AXES
    in_specs = (
        P(rows, None),
        P(rows, None),
        P(rows, None),
        P(rows, None, None),
        P(AXES, None, None),
        P(AXES, None, None),
    )
    out_specs = P(rows, None)
    return jax.shard_map(shards, mesh=fine, in_specs=in_specs, out_specs=out_specs, check_vma=False)
```

```python
import jax
import jax.numpy as jnp
import numpy as np
from jax import lax
from jax.sharding import Mesh
from jax.sharding import PartitionSpec as P

AXES = ("z", "yh", "core")
RING = 4


def expert_block(rows_in, w_first, w_second):
    features = rows_in.shape[-1]
    hidden_units = w_second.shape[0]
    flat = rows_in.reshape(-1, features)
    projected = jnp.dot(flat, w_first, preferred_element_type=jnp.float32)
    intermediate_activation = (
        jax.nn.silu(projected[:, :hidden_units]) * projected[:, hidden_units:]
    ).astype(jnp.bfloat16)
    result = jnp.dot(intermediate_activation, w_second, preferred_element_type=jnp.float32).astype(
        jnp.bfloat16
    )
    return result.reshape(rows_in.shape)


def shift_z(x, step):
    return lax.ppermute(x, "z", [(i, (i + step) % RING) for i in range(RING)])


def swap(x, axis):
    return lax.ppermute(x, axis, [(0, 1), (1, 0)])


def shards(tokens, expert_ids, gate_weights, slot_rows, w_in, w_out):
    tok_rows, features = tokens.shape
    experts = slot_rows.shape[1]
    capacity = slot_rows.shape[2]
    w_first = w_in[0]
    w_second = w_out[0]
    own_rows = slot_rows[0]
    zi = lax.axis_index("z")
    yi = lax.axis_index("yh")
    ki = lax.axis_index("core")
    n_y = 2
    blocks = RING * n_y

    meta = jnp.zeros((1, features), jnp.bfloat16)
    meta = meta.at[0, : experts * capacity].set(own_rows.reshape(-1).astype(jnp.bfloat16))
    block = jnp.concatenate([tokens, meta], axis=0)

    half = (tok_rows + 1) // 2
    partner = swap(block, "yh")
    from_below = shift_z(block, 1)
    from_above = shift_z(block, -1)
    rows = tok_rows + 1
    up = shift_z(jnp.concatenate([partner, from_below[:half]], axis=0), 1)
    down = shift_z(jnp.concatenate([partner, from_above[half:]], axis=0), -1)
    p_below = up[:rows]
    p_above = down[:rows]
    far = jnp.concatenate([up[rows:], down[rows:]], axis=0)
    p_far = swap(far, "yh")

    chip = zi * n_y + yi
    mine_e = chip * 2 + ki
    pair_e = chip * 2 + (1 - ki)
    token_iota = jnp.arange(tok_rows, dtype=jnp.int32)

    def slots_of(pieces):
        stacked = jnp.stack([arr for _, _, arr in pieces])
        toks = stacked[:, :tok_rows]
        lists = stacked[:, tok_rows, : experts * capacity].astype(jnp.int32)
        lists = lists.reshape(len(pieces), experts, capacity)
        sel = jnp.stack(
            [
                lax.dynamic_index_in_dim(lists, mine_e, axis=1, keepdims=False),
                lax.dynamic_index_in_dim(lists, pair_e, axis=1, keepdims=False),
            ],
            axis=1,
        )
        one_hot = (sel[..., None] == token_iota).astype(jnp.bfloat16)
        disp = jnp.einsum(
            "bjct,btd->bjcd", one_hot, toks, preferred_element_type=jnp.float32
        ).astype(jnp.bfloat16)
        return disp[:, 0], disp[:, 1]

    def place(into, pieces, outs):
        for i, (r, q, _) in enumerate(pieces):
            where = ((zi + r) % RING) * n_y + (yi + q) % n_y
            into = lax.dynamic_update_slice(into, outs[i : i + 1], (where, 0, 0))
        return into

    stages = [
        [(0, 0, block), (0, 1, partner), (1, 0, from_above), (3, 0, from_below)],
        [(2, 0, far), (1, 1, p_above), (3, 1, p_below)],
        [(2, 1, p_far)],
    ]
    a_abs = jnp.zeros((blocks, capacity, features), jnp.bfloat16)
    empty = a_abs
    gots = []
    for n, pieces in enumerate(stages):
        if n:
            arrs = [arr for _, _, arr in pieces]
            *arrs, a_abs = lax.optimization_barrier((*arrs, a_abs))
            pieces = [(r, q, arr) for (r, q, _), arr in zip(pieces, arrs)]
            stages[n] = pieces
        mine, got = slots_of(pieces)
        a_abs = place(a_abs, pieces, expert_block(mine, w_first, w_second))
        gots.append(got)
    ret_a = lax.all_to_all(a_abs, ("z", "yh"), 0, 0, tiled=True)
    a_abs, *gots = lax.optimization_barrier((a_abs, *gots))
    b_abs = empty
    for pieces, theirs in zip(stages, gots):
        got = swap(theirs, "core")
        b_abs = place(b_abs, pieces, swap(expert_block(got, w_first, w_second), "core"))
    ret_a, b_abs = lax.optimization_barrier((ret_a, b_abs))
    ret_b = lax.all_to_all(b_abs, ("z", "yh"), 0, 0, tiled=True)

    matches = (
        expert_ids[:, :, None] == jnp.arange(experts, dtype=jnp.int32)[None, None, :]
    ).astype(jnp.float32)
    gate_of = jnp.einsum("tk,tke->et", gate_weights, matches).astype(jnp.bfloat16)
    rows3 = own_rows.reshape(blocks, 2, capacity)
    gate3 = gate_of.reshape(blocks, 2, tok_rows)

    def contribution(which, returned):
        rows = lax.dynamic_index_in_dim(rows3, which, axis=1, keepdims=False)
        gates = lax.dynamic_index_in_dim(gate3, which, axis=1, keepdims=False)
        mixing = jnp.where(
            rows[:, :, None] == token_iota[None, None, :],
            gates[:, None, :],
            jnp.zeros((), jnp.bfloat16),
        )
        return jnp.dot(
            mixing.reshape(-1, tok_rows).T,
            returned.reshape(-1, features),
            preferred_element_type=jnp.float32,
        )

    first = contribution(ki, ret_a)
    ret_b, first = lax.optimization_barrier((ret_b, first))
    summed = first + contribution(1 - ki, ret_b)
    return summed.astype(jnp.bfloat16)


def solution(mesh):
    devices = np.asarray(mesh.devices)
    groups = devices.shape[0]
    fine = Mesh(devices.reshape(groups, RING, 2, 2), ("dp",) + AXES)
    rows = ("dp",) + AXES
    in_specs = (
        P(rows, None),
        P(rows, None),
        P(rows, None),
        P(rows, None, None),
        P(AXES, None, None),
        P(AXES, None, None),
    )
    out_specs = P(rows, None)
    return jax.shard_map(shards, mesh=fine, in_specs=in_specs, out_specs=out_specs, check_vma=False)
```

```python
import jax
import jax.numpy as jnp
import numpy as np
from jax import lax
from jax.sharding import Mesh
from jax.sharding import PartitionSpec as P

AXES = ("z", "yh", "core")
RING = 4


def expert_block(rows_in, w_first, w_second):
    features = rows_in.shape[-1]
    hidden_units = w_second.shape[0]
    flat = rows_in.reshape(-1, features)
    projected = jnp.dot(flat, w_first, preferred_element_type=jnp.float32)
    intermediate_activation = (
        jax.nn.silu(projected[:, :hidden_units]) * projected[:, hidden_units:]
    ).astype(jnp.bfloat16)
    result = jnp.dot(intermediate_activation, w_second, preferred_element_type=jnp.float32).astype(
        jnp.bfloat16
    )
    return result.reshape(rows_in.shape)


def shift_z(x, step):
    return lax.ppermute(x, "z", [(i, (i + step) % RING) for i in range(RING)])


def swap(x, axis):
    return lax.ppermute(x, axis, [(0, 1), (1, 0)])


def shards(tokens, expert_ids, gate_weights, slot_rows, w_in, w_out):
    tok_rows, features = tokens.shape
    experts = slot_rows.shape[1]
    capacity = slot_rows.shape[2]
    w_first = w_in[0]
    w_second = w_out[0]
    own_rows = slot_rows[0]
    zi = lax.axis_index("z")
    yi = lax.axis_index("yh")
    ki = lax.axis_index("core")
    n_y = 2
    blocks = RING * n_y

    meta = jnp.zeros((1, features), jnp.bfloat16)
    meta = meta.at[0, : experts * capacity].set(own_rows.reshape(-1).astype(jnp.bfloat16))
    block = jnp.concatenate([tokens, meta], axis=0)

    half = (tok_rows + 1) // 2
    partner = swap(block, "yh")
    from_below = shift_z(block, 1)
    from_above = shift_z(block, -1)
    rows = tok_rows + 1
    up = shift_z(jnp.concatenate([partner, from_below[:half]], axis=0), 1)
    down = shift_z(jnp.concatenate([partner, from_above[half:]], axis=0), -1)
    p_below = up[:rows]
    p_above = down[:rows]
    far = jnp.concatenate([up[rows:], down[rows:]], axis=0)
    p_far = jnp.concatenate([shift_z(p_below[:half], 1), shift_z(p_above[half:], -1)], axis=0)

    chip = zi * n_y + yi
    mine_e = chip * 2 + ki
    pair_e = chip * 2 + (1 - ki)
    token_iota = jnp.arange(tok_rows, dtype=jnp.int32)

    def slots_of(pieces):
        stacked = jnp.stack([arr for _, _, arr in pieces])
        toks = stacked[:, :tok_rows]
        lists = stacked[:, tok_rows, : experts * capacity].astype(jnp.int32)
        lists = lists.reshape(len(pieces), experts, capacity)
        sel = jnp.stack(
            [
                lax.dynamic_index_in_dim(lists, mine_e, axis=1, keepdims=False),
                lax.dynamic_index_in_dim(lists, pair_e, axis=1, keepdims=False),
            ],
            axis=1,
        )
        one_hot = (sel[..., None] == token_iota).astype(jnp.bfloat16)
        disp = [
            jnp.einsum(
                "bct,btd->bcd", one_hot[:, j], toks, preferred_element_type=jnp.float32
            ).astype(jnp.bfloat16)
            for j in range(2)
        ]
        return disp[0], swap(disp[1], "core")

    def place(into, pieces, outs):
        for i, (r, q, _) in enumerate(pieces):
            where = ((zi + r) % RING) * n_y + (yi + q) % n_y
            into = lax.dynamic_update_slice(into, outs[i : i + 1], (where, 0, 0))
        return into

    early = [(0, 0, block), (0, 1, partner), (1, 0, from_above), (3, 0, from_below)]
    late = [(2, 0, far), (2, 1, p_far), (1, 1, p_above), (3, 1, p_below)]
    mine_1, got_1 = slots_of(early)
    out_m1 = expert_block(mine_1, w_first, w_second)
    empty = jnp.zeros((blocks, capacity, features), jnp.bfloat16)
    a_part = place(empty, early, out_m1)
    late_arrs = [arr for _, _, arr in late]
    *late_arrs, a_part = lax.optimization_barrier((*late_arrs, a_part))
    late = [(r, q, arr) for (r, q, _), arr in zip(late, late_arrs)]
    mine_2, got_2 = slots_of(late)
    out_m2 = expert_block(mine_2, w_first, w_second)
    a_abs = place(a_part, late, out_m2)
    ret_a = lax.all_to_all(a_abs, ("z", "yh"), 0, 0, tiled=True)
    a_abs, got_1, got_2 = lax.optimization_barrier((a_abs, got_1, got_2))
    out_g1 = expert_block(got_1, w_first, w_second)
    out_g2 = expert_block(got_2, w_first, w_second)
    b_abs = place(place(empty, early, swap(out_g1, "core")), late, swap(out_g2, "core"))
    ret_a, b_abs = lax.optimization_barrier((ret_a, b_abs))
    ret_b = lax.all_to_all(b_abs, ("z", "yh"), 0, 0, tiled=True)

    matches = (
        expert_ids[:, :, None] == jnp.arange(experts, dtype=jnp.int32)[None, None, :]
    ).astype(jnp.float32)
    gate_of = jnp.einsum("tk,tke->et", gate_weights, matches).astype(jnp.bfloat16)
    rows3 = own_rows.reshape(blocks, 2, capacity)
    gate3 = gate_of.reshape(blocks, 2, tok_rows)

    def contribution(which, returned):
        rows = lax.dynamic_index_in_dim(rows3, which, axis=1, keepdims=False)
        gates = lax.dynamic_index_in_dim(gate3, which, axis=1, keepdims=False)
        mixing = jnp.where(
            rows[:, :, None] == token_iota[None, None, :],
            gates[:, None, :],
            jnp.zeros((), jnp.bfloat16),
        )
        return jnp.dot(
            mixing.reshape(-1, tok_rows).T,
            returned.reshape(-1, features),
            preferred_element_type=jnp.float32,
        )

    first = contribution(ki, ret_a)
    ret_b, first = lax.optimization_barrier((ret_b, first))
    summed = first + contribution(1 - ki, ret_b)
    return summed.astype(jnp.bfloat16)


def solution(mesh):
    devices = np.asarray(mesh.devices)
    groups = devices.shape[0]
    fine = Mesh(devices.reshape(groups, RING, 2, 2), ("dp",) + AXES)
    rows = ("dp",) + AXES
    in_specs = (
        P(rows, None),
        P(rows, None),
        P(rows, None),
        P(rows, None, None),
        P(AXES, None, None),
        P(AXES, None, None),
    )
    out_specs = P(rows, None)
    return jax.shard_map(shards, mesh=fine, in_specs=in_specs, out_specs=out_specs, check_vma=False)
```

```python
import jax
import jax.numpy as jnp
import numpy as np
from jax import lax
from jax.sharding import Mesh
from jax.sharding import PartitionSpec as P

AXES = ("z", "yh", "core")
RING = 4


def expert_block(rows_in, w_first, w_second):
    features = rows_in.shape[-1]
    hidden_units = w_second.shape[0]
    flat = rows_in.reshape(-1, features)
    projected = jnp.dot(flat, w_first, preferred_element_type=jnp.float32)
    intermediate_activation = (
        jax.nn.silu(projected[:, :hidden_units]) * projected[:, hidden_units:]
    ).astype(jnp.bfloat16)
    result = jnp.dot(intermediate_activation, w_second, preferred_element_type=jnp.float32).astype(
        jnp.bfloat16
    )
    return result.reshape(rows_in.shape)


def shift_z(x, step):
    return lax.ppermute(x, "z", [(i, (i + step) % RING) for i in range(RING)])


def swap(x, axis):
    return lax.ppermute(x, axis, [(0, 1), (1, 0)])


def shards(tokens, expert_ids, gate_weights, slot_rows, w_in, w_out):
    tok_rows, features = tokens.shape
    experts = slot_rows.shape[1]
    capacity = slot_rows.shape[2]
    w_first = w_in[0]
    w_second = w_out[0]
    own_rows = slot_rows[0]
    zi = lax.axis_index("z")
    yi = lax.axis_index("yh")
    ki = lax.axis_index("core")
    n_y = 2
    blocks = RING * n_y

    meta = jnp.concatenate(
        [
            own_rows.reshape(1, -1).astype(jnp.bfloat16),
            jnp.zeros((1, features - experts * capacity), jnp.bfloat16),
        ],
        axis=1,
    )
    block = jnp.concatenate([tokens, meta], axis=0)

    half = (tok_rows + 1) // 2
    partner = swap(block, "yh")
    from_below = shift_z(block, 1)
    from_above = shift_z(block, -1)
    rows = tok_rows + 1
    up = shift_z(jnp.concatenate([partner, from_below[:half]], axis=0), 1)
    down = shift_z(jnp.concatenate([partner, from_above[half:]], axis=0), -1)
    p_below = up[:rows]
    p_above = down[:rows]
    far = jnp.concatenate([up[rows:], down[rows:]], axis=0)
    p_far = jnp.concatenate([shift_z(p_below[:half], 1), shift_z(p_above[half:], -1)], axis=0)

    chip = zi * n_y + yi
    mine_e = chip * 2 + ki
    pair_e = chip * 2 + (1 - ki)
    token_iota = jnp.arange(tok_rows, dtype=jnp.int32)

    def slots_of(pieces):
        stacked = jnp.stack([arr for _, _, arr in pieces])
        toks = stacked[:, :tok_rows]
        lists = stacked[:, tok_rows, : experts * capacity].astype(jnp.int32)
        lists = lists.reshape(len(pieces), experts, capacity)
        sel = jnp.stack(
            [
                lax.dynamic_index_in_dim(lists, mine_e, axis=1, keepdims=False),
                lax.dynamic_index_in_dim(lists, pair_e, axis=1, keepdims=False),
            ],
            axis=1,
        )
        one_hot = (sel[..., None] == token_iota).astype(jnp.bfloat16)
        disp = [
            jnp.einsum(
                "bct,btd->bcd", one_hot[:, j], toks, preferred_element_type=jnp.float32
            ).astype(jnp.bfloat16)
            for j in range(2)
        ]
        return disp[0], swap(disp[1], "core")

    def place(into, pieces, outs):
        for i, (r, q, _) in enumerate(pieces):
            where = ((zi + r) % RING) * n_y + (yi + q) % n_y
            into = lax.dynamic_update_slice(into, outs[i : i + 1], (where, 0, 0))
        return into

    early = [(0, 0, block), (0, 1, partner), (1, 0, from_above), (3, 0, from_below)]
    late = [(2, 0, far), (2, 1, p_far), (1, 1, p_above), (3, 1, p_below)]
    mine_1, got_1 = slots_of(early)
    out_m1 = expert_block(mine_1, w_first, w_second)
    empty = jnp.zeros((blocks, capacity, features), jnp.bfloat16)
    a_part = place(empty, early, out_m1)
    late_arrs = [arr for _, _, arr in late]
    *late_arrs, a_part = lax.optimization_barrier((*late_arrs, a_part))
    late = [(r, q, arr) for (r, q, _), arr in zip(late, late_arrs)]
    mine_2, got_2 = slots_of(late)
    out_m2 = expert_block(mine_2, w_first, w_second)
    a_abs = place(a_part, late, out_m2)
    ret_a = lax.all_to_all(a_abs, ("z", "yh"), 0, 0, tiled=True)
    a_abs, got_1, got_2 = lax.optimization_barrier((a_abs, got_1, got_2))
    out_g1 = expert_block(got_1, w_first, w_second)
    out_g2 = expert_block(got_2, w_first, w_second)
    b_abs = place(place(empty, early, swap(out_g1, "core")), late, swap(out_g2, "core"))
    ret_a, b_abs = lax.optimization_barrier((ret_a, b_abs))
    ret_b = lax.all_to_all(b_abs, ("z", "yh"), 0, 0, tiled=True)

    matches = (
        expert_ids[:, :, None] == jnp.arange(experts, dtype=jnp.int32)[None, None, :]
    ).astype(jnp.float32)
    gate_of = jnp.einsum("tk,tke->et", gate_weights, matches).astype(jnp.bfloat16)
    rows3 = own_rows.reshape(blocks, 2, capacity)
    gate3 = gate_of.reshape(blocks, 2, tok_rows)

    def contribution(which, returned):
        rows = lax.dynamic_index_in_dim(rows3, which, axis=1, keepdims=False)
        gates = lax.dynamic_index_in_dim(gate3, which, axis=1, keepdims=False)
        mixing = jnp.where(
            rows[:, :, None] == token_iota[None, None, :],
            gates[:, None, :],
            jnp.zeros((), jnp.bfloat16),
        )
        return jnp.dot(
            mixing.reshape(-1, tok_rows).T,
            returned.reshape(-1, features),
            preferred_element_type=jnp.float32,
        )

    first = contribution(ki, ret_a)
    ret_b, first = lax.optimization_barrier((ret_b, first))
    summed = first + contribution(1 - ki, ret_b)
    return summed.astype(jnp.bfloat16)


def solution(mesh):
    devices = np.asarray(mesh.devices)
    groups = devices.shape[0]
    fine = Mesh(devices.reshape(groups, RING, 2, 2), ("dp",) + AXES)
    rows = ("dp",) + AXES
    in_specs = (
        P(rows, None),
        P(rows, None),
        P(rows, None),
        P(rows, None, None),
        P(AXES, None, None),
        P(AXES, None, None),
    )
    out_specs = P(rows, None)
    return jax.shard_map(shards, mesh=fine, in_specs=in_specs, out_specs=out_specs, check_vma=False)
```

```python
import jax
import jax.numpy as jnp
import numpy as np
from jax import lax
from jax.sharding import Mesh
from jax.sharding import PartitionSpec as P

AXES = ("z", "yh", "core")
RING = 4


def expert_block(rows_in, w_first, w_second):
    features = rows_in.shape[-1]
    hidden_units = w_second.shape[0]
    flat = rows_in.reshape(-1, features)
    projected = jnp.dot(flat, w_first, preferred_element_type=jnp.float32)
    intermediate_activation = (
        jax.nn.silu(projected[:, :hidden_units]) * projected[:, hidden_units:]
    ).astype(jnp.bfloat16)
    result = jnp.dot(intermediate_activation, w_second, preferred_element_type=jnp.float32).astype(
        jnp.bfloat16
    )
    return result.reshape(rows_in.shape)


def shift_z(x, step):
    return lax.ppermute(x, "z", [(i, (i + step) % RING) for i in range(RING)])


def swap(x, axis):
    return lax.ppermute(x, axis, [(0, 1), (1, 0)])


def shards(tokens, expert_ids, gate_weights, slot_rows, w_in, w_out):
    tok_rows, features = tokens.shape
    experts = slot_rows.shape[1]
    capacity = slot_rows.shape[2]
    w_first = w_in[0]
    w_second = w_out[0]
    own_rows = slot_rows[0]
    zi = lax.axis_index("z")
    yi = lax.axis_index("yh")
    ki = lax.axis_index("core")
    n_y = 2
    blocks = RING * n_y

    meta = jnp.concatenate(
        [
            own_rows.reshape(1, -1).astype(jnp.bfloat16),
            jnp.zeros((1, features - experts * capacity), jnp.bfloat16),
        ],
        axis=1,
    )
    block = jnp.concatenate([tokens, meta], axis=0)

    half = (tok_rows + 1) // 2
    partner = swap(block, "yh")
    from_below = shift_z(block, 1)
    from_above = shift_z(block, -1)
    rows = tok_rows + 1
    up = shift_z(jnp.concatenate([partner, from_below[:half]], axis=0), 1)
    down = shift_z(jnp.concatenate([partner, from_above[half:]], axis=0), -1)
    p_below = up[:rows]
    p_above = down[:rows]
    far = jnp.concatenate([up[rows:], down[rows:]], axis=0)
    p_far = jnp.concatenate([shift_z(p_below[:half], 1), shift_z(p_above[half:], -1)], axis=0)

    chip = zi * n_y + yi
    mine_e = chip * 2 + ki
    pair_e = chip * 2 + (1 - ki)
    token_iota = jnp.arange(tok_rows, dtype=jnp.int32)

    def slots_of(pieces):
        stacked = jnp.stack([arr for _, _, arr in pieces])
        toks = stacked[:, :tok_rows]
        lists = stacked[:, tok_rows, : experts * capacity].astype(jnp.int32)
        lists = lists.reshape(len(pieces), experts, capacity)
        sel = jnp.stack(
            [
                lax.dynamic_index_in_dim(lists, mine_e, axis=1, keepdims=False),
                lax.dynamic_index_in_dim(lists, pair_e, axis=1, keepdims=False),
            ],
            axis=1,
        )
        one_hot = (sel[..., None] == token_iota).astype(jnp.bfloat16)
        disp = [
            jnp.einsum(
                "bct,btd->bcd", one_hot[:, j], toks, preferred_element_type=jnp.float32
            ).astype(jnp.bfloat16)
            for j in range(2)
        ]
        return disp[0], swap(disp[1], "core")

    def place(into, pieces, outs):
        for i, (r, q, _) in enumerate(pieces):
            where = ((zi + r) % RING) * n_y + (yi + q) % n_y
            into = lax.dynamic_update_slice(into, outs[i : i + 1], (where, 0, 0))
        return into

    early = [(0, 0, block), (0, 1, partner), (1, 0, from_above), (3, 0, from_below)]
    late = [(2, 0, far), (2, 1, p_far), (1, 1, p_above), (3, 1, p_below)]
    mine_1, got_1 = slots_of(early)
    out_m1 = expert_block(mine_1, w_first, w_second)
    empty = jnp.zeros((blocks, capacity, features), jnp.bfloat16)
    a_part = place(empty, early, out_m1)
    late_arrs = [arr for _, _, arr in late]
    *late_arrs, a_part = lax.optimization_barrier((*late_arrs, a_part))
    late = [(r, q, arr) for (r, q, _), arr in zip(late, late_arrs)]
    mine_2, got_2 = slots_of(late)
    out_m2 = expert_block(mine_2, w_first, w_second)
    dest = jnp.stack([((zi + r) % RING) * n_y + (yi + q) % n_y for r, q, _ in late])
    onto = (jnp.arange(blocks, dtype=jnp.int32)[:, None] == dest[None, :]).astype(jnp.bfloat16)
    a_abs = (
        a_part.astype(jnp.float32)
        + jnp.einsum("jb,bcd->jcd", onto, out_m2, preferred_element_type=jnp.float32)
    ).astype(jnp.bfloat16)
    ret_a = lax.all_to_all(a_abs, ("z", "yh"), 0, 0, tiled=True)
    a_abs, got_1, got_2 = lax.optimization_barrier((a_abs, got_1, got_2))
    out_g1 = expert_block(got_1, w_first, w_second)
    out_g2 = expert_block(got_2, w_first, w_second)
    b_abs = place(place(empty, early, swap(out_g1, "core")), late, swap(out_g2, "core"))
    ret_a, b_abs = lax.optimization_barrier((ret_a, b_abs))
    ret_b = lax.all_to_all(b_abs, ("z", "yh"), 0, 0, tiled=True)

    matches = (
        expert_ids[:, :, None] == jnp.arange(experts, dtype=jnp.int32)[None, None, :]
    ).astype(jnp.float32)
    gate_of = jnp.einsum("tk,tke->et", gate_weights, matches).astype(jnp.bfloat16)
    rows3 = own_rows.reshape(blocks, 2, capacity)
    gate3 = gate_of.reshape(blocks, 2, tok_rows)

    def contribution(which, returned):
        rows = lax.dynamic_index_in_dim(rows3, which, axis=1, keepdims=False)
        gates = lax.dynamic_index_in_dim(gate3, which, axis=1, keepdims=False)
        mixing = jnp.where(
            rows[:, :, None] == token_iota[None, None, :],
            gates[:, None, :],
            jnp.zeros((), jnp.bfloat16),
        )
        return jnp.dot(
            mixing.reshape(-1, tok_rows).T,
            returned.reshape(-1, features),
            preferred_element_type=jnp.float32,
        )

    first = contribution(ki, ret_a)
    ret_b, first = lax.optimization_barrier((ret_b, first))
    summed = first + contribution(1 - ki, ret_b)
    return summed.astype(jnp.bfloat16)


def solution(mesh):
    devices = np.asarray(mesh.devices)
    groups = devices.shape[0]
    fine = Mesh(devices.reshape(groups, RING, 2, 2), ("dp",) + AXES)
    rows = ("dp",) + AXES
    in_specs = (
        P(rows, None),
        P(rows, None),
        P(rows, None),
        P(rows, None, None),
        P(AXES, None, None),
        P(AXES, None, None),
    )
    out_specs = P(rows, None)
    return jax.shard_map(shards, mesh=fine, in_specs=in_specs, out_specs=out_specs, check_vma=False)
```

```python
import jax
import jax.numpy as jnp
import numpy as np
from jax import lax
from jax.sharding import Mesh
from jax.sharding import PartitionSpec as P

AXES = ("z", "yh", "core")
RING = 4


def expert_block(rows_in, w_first, w_second):
    features = rows_in.shape[-1]
    hidden_units = w_second.shape[0]
    flat = rows_in.reshape(-1, features)
    projected = jnp.dot(flat, w_first, preferred_element_type=jnp.float32)
    intermediate_activation = (
        jax.nn.silu(projected[:, :hidden_units]) * projected[:, hidden_units:]
    ).astype(jnp.bfloat16)
    result = jnp.dot(intermediate_activation, w_second, preferred_element_type=jnp.float32).astype(
        jnp.bfloat16
    )
    return result.reshape(rows_in.shape)


def shift_z(x, step):
    return lax.ppermute(x, "z", [(i, (i + step) % RING) for i in range(RING)])


def swap(x, axis):
    return lax.ppermute(x, axis, [(0, 1), (1, 0)])


def shards(tokens, expert_ids, gate_weights, slot_rows, w_in, w_out):
    tok_rows, features = tokens.shape
    experts = slot_rows.shape[1]
    capacity = slot_rows.shape[2]
    w_first = w_in[0]
    w_second = w_out[0]
    own_rows = slot_rows[0]
    zi = lax.axis_index("z")
    yi = lax.axis_index("yh")
    ki = lax.axis_index("core")
    n_y = 2
    blocks = RING * n_y

    meta = jnp.concatenate(
        [
            own_rows.reshape(1, -1).astype(jnp.bfloat16),
            jnp.zeros((1, features - experts * capacity), jnp.bfloat16),
        ],
        axis=1,
    )
    block = jnp.concatenate([tokens, meta], axis=0)

    half = (tok_rows + 1) // 2
    partner = swap(block, "yh")
    from_below = shift_z(block, 1)
    from_above = shift_z(block, -1)
    rows = tok_rows + 1
    up = shift_z(jnp.concatenate([partner, from_below[:half]], axis=0), 1)
    down = shift_z(jnp.concatenate([partner, from_above[half:]], axis=0), -1)
    p_below = up[:rows]
    p_above = down[:rows]
    far = jnp.concatenate([up[rows:], down[rows:]], axis=0)
    p_far = jnp.concatenate([shift_z(p_below[:half], 1), shift_z(p_above[half:], -1)], axis=0)

    chip = zi * n_y + yi
    mine_e = chip * 2 + ki
    pair_e = chip * 2 + (1 - ki)
    token_iota = jnp.arange(tok_rows, dtype=jnp.int32)

    def slots_of(pieces):
        stacked = jnp.stack([arr for _, _, arr in pieces])
        toks = stacked[:, :tok_rows]
        lists = stacked[:, tok_rows, : experts * capacity].astype(jnp.int32)
        lists = lists.reshape(len(pieces), experts, capacity)
        sel = jnp.stack(
            [
                lax.dynamic_index_in_dim(lists, mine_e, axis=1, keepdims=False),
                lax.dynamic_index_in_dim(lists, pair_e, axis=1, keepdims=False),
            ],
            axis=1,
        )
        one_hot = (sel[..., None] == token_iota).astype(jnp.bfloat16)
        disp = [
            jnp.einsum(
                "bct,btd->bcd", one_hot[:, j], toks, preferred_element_type=jnp.float32
            ).astype(jnp.bfloat16)
            for j in range(2)
        ]
        return disp[0], swap(disp[1], "core")

    def place(into, pieces, outs):
        for i, (r, q, _) in enumerate(pieces):
            where = ((zi + r) % RING) * n_y + (yi + q) % n_y
            into = lax.dynamic_update_slice(into, outs[i : i + 1], (where, 0, 0))
        return into

    own, partner = lax.optimization_barrier((block, partner))
    early = [(0, 0, own), (0, 1, partner), (1, 0, from_above), (3, 0, from_below)]
    late = [(2, 0, far), (2, 1, p_far), (1, 1, p_above), (3, 1, p_below)]
    mine_1, got_1 = slots_of(early)
    out_m1 = expert_block(mine_1, w_first, w_second)
    empty = jnp.zeros((blocks, capacity, features), jnp.bfloat16)
    a_part = place(empty, early, out_m1)
    late_arrs = [arr for _, _, arr in late]
    *late_arrs, a_part = lax.optimization_barrier((*late_arrs, a_part))
    late = [(r, q, arr) for (r, q, _), arr in zip(late, late_arrs)]
    mine_2, got_2 = slots_of(late)
    out_m2 = expert_block(mine_2, w_first, w_second)
    a_abs = place(a_part, late, out_m2)
    ret_a = lax.all_to_all(a_abs, ("z", "yh"), 0, 0, tiled=True)
    a_abs, got_1, got_2 = lax.optimization_barrier((a_abs, got_1, got_2))
    out_g1 = expert_block(got_1, w_first, w_second)
    out_g2 = expert_block(got_2, w_first, w_second)
    b_abs = place(place(empty, early, swap(out_g1, "core")), late, swap(out_g2, "core"))
    ret_a, b_abs = lax.optimization_barrier((ret_a, b_abs))
    ret_b = lax.all_to_all(b_abs, ("z", "yh"), 0, 0, tiled=True)

    matches = (
        expert_ids[:, :, None] == jnp.arange(experts, dtype=jnp.int32)[None, None, :]
    ).astype(jnp.float32)
    gate_of = jnp.einsum("tk,tke->et", gate_weights, matches).astype(jnp.bfloat16)
    rows3 = own_rows.reshape(blocks, 2, capacity)
    gate3 = gate_of.reshape(blocks, 2, tok_rows)

    def contribution(which, returned):
        rows = lax.dynamic_index_in_dim(rows3, which, axis=1, keepdims=False)
        gates = lax.dynamic_index_in_dim(gate3, which, axis=1, keepdims=False)
        mixing = jnp.where(
            rows[:, :, None] == token_iota[None, None, :],
            gates[:, None, :],
            jnp.zeros((), jnp.bfloat16),
        )
        return jnp.dot(
            mixing.reshape(-1, tok_rows).T,
            returned.reshape(-1, features),
            preferred_element_type=jnp.float32,
        )

    first = contribution(ki, ret_a)
    ret_b, first = lax.optimization_barrier((ret_b, first))
    summed = first + contribution(1 - ki, ret_b)
    return summed.astype(jnp.bfloat16)


def solution(mesh):
    devices = np.asarray(mesh.devices)
    groups = devices.shape[0]
    fine = Mesh(devices.reshape(groups, RING, 2, 2), ("dp",) + AXES)
    rows = ("dp",) + AXES
    in_specs = (
        P(rows, None),
        P(rows, None),
        P(rows, None),
        P(rows, None, None),
        P(AXES, None, None),
        P(AXES, None, None),
    )
    out_specs = P(rows, None)
    return jax.shard_map(shards, mesh=fine, in_specs=in_specs, out_specs=out_specs, check_vma=False)
```
